256 devices in a mesh: section: 2 (over x_hi), ctx: 32 (over z, x_lo, core), mp: 4 (over y).
Axes of the slice: x: 4 (x_hi: 2, x_lo: 2; x = x_hi * 2 + x_lo), y: 4, z: 8, core: 2. Of those that a mesh axis runs over, the one named last changes fastest.
Arguments:
- queries: bfloat16 [2, 8192, 4096], P('section', 'ctx', 'mp'), may hold values from -130 to 130
- keys: bfloat16 [2, 8192, 512], P('section', 'ctx', 'mp'), may hold values from -4.5 to 4.5
- values: bfloat16 [2, 8192, 512], P('section', 'ctx', 'mp'), may hold values from -6 to 6
- doc_lengths: int32 [2, 16], P('section'), may hold values from 1 to 4096, 8192 in all within a row
Outputs:
- attended: bfloat16 [2, 8192, 4096], P('section', ('ctx', 'mp'))
- passed: bfloat16 [2, 8192, 4096], P('section', ('ctx', 'mp'))
The draws below stay inside these ranges and needn't reach their ends.
All inputs are finite; a program needn't handle non-finite values.
Results may differ from the reference program's by a relative error of at most 0.004.
Values may be sent and summed in bfloat16 or wider, within the bound.
No kernel may reach another device: no remote copies, remote signals or barrier semaphores. Data moves between devices by JAX's collectives and lax.ppermute only.
A program may use at most 192 MiB of HBM per device.

```python
import math
import jax
import jax.numpy as jnp
import numpy as np
from jax import lax

DH = 128
QH = 32
KVH = 4
DOCS = 16
SECTIONS = 2
TOKENS = 8192
MOST = 4096
LOGN_BASE = 512


def shared_rows(key):
    base = jax.random.fold_in(key, 11)
    first = jax.random.fold_in(base, 0)
    key_base = jnp.clip(jax.random.normal(first, (SECTIONS, TOKENS, KVH, DH), jnp.float32), -4.0, 4.0)
    final_keys = key_base
    return final_keys


def draw_keys(key, part):
    final_keys = shared_rows(key)
    return final_keys.reshape(SECTIONS, TOKENS, KVH * DH).astype(jnp.bfloat16)


def draw_queries(key, part):
    query_key = jax.random.fold_in(key, 23)
    query_base = jnp.clip(jax.random.normal(query_key, (SECTIONS, TOKENS, QH, DH), jnp.float32), -6.0, 6.0)
    result = query_base
    return result.reshape(SECTIONS, TOKENS, QH * DH).astype(jnp.bfloat16)


def block_levels(own_key, dims, cuts, least, largest):
    loudness, own = 1.0, jax.random.fold_in(own_key, 6)
    for position, shards_of in cuts:
        heights = jnp.exp(jax.random.uniform(jax.random.fold_in(own, position), (shards_of,), jnp.float32, least / len(cuts), largest / len(cuts)))
        loudness = loudness * jnp.repeat(heights, dims[position] // shards_of).reshape([-1 if axis == position else 1 for axis in range(len(dims))])
    return loudness


def length_profile(count, total, bound, skew):
    loads = [(1 << 20) // math.isqrt(standing ** skew) + 1 for standing in range(2, count + 1)]
    surplus, counts = total - bound - (count - 1), [1] * (count - 1)
    while surplus > 0:
        free = [i for i in range(count - 1) if counts[i] < bound]
        mass, budget = sum([loads[i] for i in free]), surplus
        for i in free:
            extra = min(bound - counts[i], max(1, budget * loads[i] // mass), surplus)
            counts[i] = counts[i] + extra
            surplus = surplus - extra
    return np.array([bound] + counts)


def uneven(own_key, number_of, total, limit, slope):
    if number_of == 2:
        one = jax.random.randint(own_key, (), max(1, total - limit), min(limit, total - 1) + 1)
        return jnp.stack([one, total - one])
    sizes = jnp.asarray(length_profile(number_of, total, limit, slope), jnp.int32)
    pairs = (number_of - 1) // 2
    giver, sink = sizes[1:1 + 2 * pairs:2], sizes[2:2 + 2 * pairs:2]
    margin = jnp.minimum(giver - 1, limit - sink)
    moved = jax.random.randint(jax.random.fold_in(own_key, 1), (pairs,), 0, 1 << 20) % (margin + 1)
    sizes = sizes.at[1:1 + 2 * pairs:2].set(giver - moved).at[2:2 + 2 * pairs:2].set(sink + moved)
    return sizes[jax.random.permutation(jax.random.fold_in(own_key, 2), number_of)]


def normal_values(own_key, dims, spread, reach, cuts=(), held_as=jnp.bfloat16):
    level = block_levels(own_key, dims, cuts, -0.22, 0.18) if cuts else 1.0
    drawn = jax.random.normal(own_key, dims, jnp.float32) * spread * level
    return jnp.minimum(jnp.maximum(drawn, -reach), reach).astype(held_as)


def setup_inputs(seed: int = 0) -> dict:
    streams_of = jax.random.split(jax.random.key(seed), 5)
    queries = draw_queries(jax.random.fold_in(streams_of[4], 71), 0)
    keys = draw_keys(jax.random.fold_in(streams_of[4], 71), 0)
    values = normal_values(streams_of[2], (SECTIONS, TOKENS, KVH * DH), 1.0, 6.0, ((0, 2), (1, 32), (2, 4)))
    doc_lengths = jax.vmap(lambda own: uneven(own, DOCS, TOKENS, MOST, 2))(jax.random.split(streams_of[3], SECTIONS)).reshape((SECTIONS, DOCS)).astype(jnp.int32)
    return {"queries": queries, "keys": keys, "values": values, "doc_lengths": doc_lengths}


def one_section(query_rows, key_rows, value_rows, lengths):
    group = QH // KVH
    ends = jnp.cumsum(lengths).astype(jnp.int32)
    positions = jnp.arange(TOKENS, dtype=jnp.int32)
    doc = lax.optimization_barrier(jnp.sum((positions[:, None] >= ends[None, :]).astype(jnp.int32), axis=1)).astype(jnp.int32)
    doc_len = lengths[doc].astype(jnp.float32)
    scale = jnp.maximum(1.0, jnp.log(doc_len) / math.log(float(LOGN_BASE)))
    queries = query_rows.reshape(TOKENS, KVH, group, DH)
    keys_f = key_rows.reshape(TOKENS, KVH, DH).astype(jnp.float32)
    values_f = value_rows.reshape(TOKENS, KVH, DH).astype(jnp.float32)
    block = min(TOKENS, 256)
    inv = 1.0 / math.sqrt(DH)

    def one_block(index):
        start = (index * block).astype(jnp.int32)
        query_block = lax.dynamic_slice_in_dim(queries, start, block, 0).astype(jnp.float32)
        pos_block = lax.dynamic_slice_in_dim(positions, start, block, 0)
        doc_block = lax.dynamic_slice_in_dim(doc, start, block, 0)
        scale_block = lax.dynamic_slice_in_dim(scale, start, block, 0)
        score = jnp.einsum('qhgd,khd->hgqk', query_block, keys_f)
        score = score * (scale_block * inv)[None, None, :, None]
        allowed = (doc_block[:, None] == doc[None, :]) & (positions[None, :] <= pos_block[:, None])
        score = jnp.where(allowed[None, None], score, -1e+30)
        top = lax.optimization_barrier(jnp.max(score, axis=-1, keepdims=True))
        weight = jnp.where(allowed[None, None], jnp.exp(score - top), 0.0)
        total = lax.optimization_barrier(jnp.sum(weight, axis=-1))
        rounded = lax.optimization_barrier(weight.astype(jnp.bfloat16)).astype(jnp.float32)
        summed = jnp.einsum('hgqk,khd->qhgd', rounded, values_f)
        result = summed / jnp.transpose(total, (2, 0, 1))[..., None]
        return result.astype(jnp.bfloat16).reshape(block, QH * DH)
    blocks = lax.map(one_block, jnp.arange(TOKENS // block, dtype=jnp.int32))
    return blocks.reshape(TOKENS, QH * DH)

def reference(queries, keys, values, doc_lengths):
    outputs = []
    for section in range(SECTIONS):
        outputs.append(one_section(queries[section], keys[section], values[section], doc_lengths[section]))
    attended = jnp.stack(outputs, axis=0)
    passed = jnp.roll(attended, 1, axis=0)
    return (attended, passed)
```

```python
import functools
import math

import jax
import jax.numpy as jnp
from jax import lax
from jax.experimental import pallas as pl
from jax.experimental.pallas import tpu as pltpu
from jax.sharding import PartitionSpec as P

DH = 128
DOCS = 16
MOST = 4096
BK = 512


def from_behind(block, axis, distance):
    devices = range(lax.axis_size(axis))
    route = [((i - distance) % len(devices), i) for i in devices]
    return lax.ppermute(block, axis, route)


def doc_of(positions, ends):
    return jnp.sum((positions[:, None] >= ends[None, :]).astype(jnp.int32), axis=1)


def flash_kernel(bounds_ref, q_ref, kv_ref, qdoc_ref, qpos_ref, fac_ref, kdoc_ref,
                 o_ref, m_sc, l_sc, acc_sc, *, heads, bk, steps):
    j = pl.program_id(0)
    lo = bounds_ref[0]
    hi = bounds_ref[1]

    @pl.when(j == 0)
    def _():
        m_sc[...] = jnp.full(m_sc.shape, -1e30, jnp.float32)
        l_sc[...] = jnp.zeros(l_sc.shape, jnp.float32)
        acc_sc[...] = jnp.zeros(acc_sc.shape, jnp.float32)

    blk = lo + j

    @pl.when(blk <= hi)
    def _():
        k = kv_ref[:, :DH]
        v = kv_ref[:, DH:]
        kpos = blk * bk + lax.broadcasted_iota(jnp.int32, (1, bk), 1)
        allowed = (qdoc_ref[...] == kdoc_ref[...]) & (kpos <= qpos_ref[...])
        fac = fac_ref[...]
        for h in range(heads):
            q = q_ref[:, h * DH:(h + 1) * DH]
            s = lax.dot_general(q, k, (((1,), (1,)), ((), ())),
                                preferred_element_type=jnp.float32)
            s = jnp.where(allowed, s * fac, -1e30)
            m_old = m_sc[h]
            m_new = jnp.maximum(m_old, jnp.max(s, axis=1, keepdims=True))
            alpha = jnp.exp(m_old - m_new)
            p = jnp.where(allowed, jnp.exp(s - m_new), 0.0)
            l_sc[h] = alpha * l_sc[h] + jnp.sum(p, axis=1, keepdims=True)
            pv = lax.dot_general(p.astype(jnp.bfloat16), v, (((1,), (0,)), ((), ())),
                                 preferred_element_type=jnp.float32)
            acc_sc[h] = alpha * acc_sc[h] + pv
            m_sc[h] = m_new

    @pl.when(j == steps - 1)
    def _():
        for h in range(heads):
            o_ref[:, h * DH:(h + 1) * DH] = (acc_sc[h] / l_sc[h]).astype(o_ref.dtype)


def attend(bounds, query_rows, kv, query_doc, query_pos, factor, key_doc, steps, bk):
    rows, width = query_rows.shape
    heads = width // DH

    def kv_map(j, b):
        return (jnp.minimum(b[0] + j, b[1]), 0)

    def kdoc_map(j, b):
        return (0, jnp.minimum(b[0] + j, b[1]))

    whole = lambda j, b: (0, 0)
    return pl.pallas_call(
        functools.partial(flash_kernel, heads=heads, bk=bk, steps=steps),
        out_shape=jax.ShapeDtypeStruct((rows, width), jnp.bfloat16),
        grid_spec=pltpu.PrefetchScalarGridSpec(
            num_scalar_prefetch=1,
            grid=(steps,),
            in_specs=[
                pl.BlockSpec((rows, width), whole),
                pl.BlockSpec((bk, 2 * DH), kv_map),
                pl.BlockSpec((rows, 1), whole),
                pl.BlockSpec((rows, 1), whole),
                pl.BlockSpec((rows, 1), whole),
                pl.BlockSpec((1, bk), kdoc_map),
            ],
            out_specs=pl.BlockSpec((rows, width), whole),
            scratch_shapes=[
                pltpu.VMEM((heads, rows, 1), jnp.float32),
                pltpu.VMEM((heads, rows, 1), jnp.float32),
                pltpu.VMEM((heads, rows, DH), jnp.float32),
            ],
        ),
        compiler_params=pltpu.CompilerParams(dimension_semantics=("arbitrary",)),
    )(bounds, query_rows, kv, query_doc, query_pos, factor, key_doc)


def body(queries, keys, values, doc_lengths):
    query_rows = queries[0]
    key_rows = keys[0]
    value_rows = values[0]
    lengths = doc_lengths[0]
    rows = query_rows.shape[0]
    cycle = lax.axis_size("ctx")
    count = rows * cycle
    base_len = count // 16
    position = lax.axis_index("ctx")
    first = position * rows
    ends = jnp.cumsum(lengths)
    starts = ends - lengths
    query_pos = first + jnp.arange(rows, dtype=jnp.int32)
    query_doc = doc_of(query_pos, ends)
    lookup = query_doc[:, None] == jnp.arange(DOCS, dtype=jnp.int32)[None, :]
    query_len = jnp.sum(jnp.where(lookup, lengths[None, :], 0), axis=1).astype(jnp.float32)
    factor = jnp.maximum(1.0, jnp.log(query_len) / math.log(float(base_len))) * (
        1.0 / math.sqrt(DH)
    )
    bk = min(BK, count)
    span = max(
        (c * rows + rows - 1) // bk - max(0, c * rows - (MOST - 1)) // bk + 1
        for c in range(cycle)
    )
    first_doc = jnp.sum((first >= ends).astype(jnp.int32))
    lo = jnp.sum(jnp.where(jnp.arange(DOCS) == first_doc, starts, 0)) // bk
    hi = (first + rows - 1) // bk
    bounds = jnp.stack([lo, hi]).astype(jnp.int32)
    kv_rows = jnp.concatenate([key_rows, value_rows], axis=1)
    kv = lax.all_gather(kv_rows, "ctx", axis=0, tiled=True)
    key_doc = doc_of(jnp.arange(count, dtype=jnp.int32), ends)[None, :]
    result = attend(
        bounds, query_rows, kv, query_doc[:, None], query_pos[:, None], factor[:, None],
        key_doc, span, bk,
    )
    own = lax.all_to_all(result, "mp", split_axis=0, concat_axis=1, tiled=True)
    moved = from_behind(own, "section", 1)
    return (own[None], moved[None])


def solution(mesh):
    return jax.shard_map(
        body,
        mesh=mesh,
        in_specs=(
            P("section", "ctx", "mp"),
            P("section", "ctx", "mp"),
            P("section", "ctx", "mp"),
            P("section", None),
        ),
        out_specs=(P("section", ("ctx", "mp"), None), P("section", ("ctx", "mp"), None)),
        check_vma=False,
    )
```

```python
import functools
import math

import jax
import jax.numpy as jnp
from jax import lax
from jax.experimental import pallas as pl
from jax.experimental.pallas import tpu as pltpu
from jax.sharding import PartitionSpec as P

DH = 128
DOCS = 16
MOST = 4096
BK = 512


def from_behind(block, axis, distance):
    devices = range(lax.axis_size(axis))
    route = [((i - distance) % len(devices), i) for i in devices]
    return lax.ppermute(block, axis, route)


def doc_of(positions, ends):
    return jnp.sum((positions[:, None] >= ends[None, :]).astype(jnp.int32), axis=1)


def flash_kernel(bounds_ref, q_ref, kv_ref, qdoc_ref, qpos_ref, fac_ref, kdoc_ref,
                 o_ref, m_sc, l_sc, acc_sc, *, heads, bk, steps):
    j = pl.program_id(0)
    lo = bounds_ref[0]
    hi = bounds_ref[1]

    @pl.when(j == 0)
    def _():
        m_sc[...] = jnp.full(m_sc.shape, -1e30, jnp.float32)
        l_sc[...] = jnp.zeros(l_sc.shape, jnp.float32)
        acc_sc[...] = jnp.zeros(acc_sc.shape, jnp.float32)

    blk = lo + j
    full = bounds_ref[2 + j] == 1

    def step(masked):
        k = kv_ref[:, :DH]
        v = kv_ref[:, DH:]
        if masked:
            kpos = blk * bk + lax.broadcasted_iota(jnp.int32, (1, bk), 1)
            allowed = (qdoc_ref[...] == kdoc_ref[...]) & (kpos <= qpos_ref[...])
        fac = fac_ref[...]
        for h in range(heads):
            q = q_ref[:, h * DH:(h + 1) * DH]
            s = lax.dot_general(q, k, (((1,), (1,)), ((), ())),
                                preferred_element_type=jnp.float32)
            s = s * fac
            if masked:
                s = jnp.where(allowed, s, -1e30)
            m_old = m_sc[h]
            m_new = jnp.maximum(m_old, jnp.max(s, axis=1, keepdims=True))
            alpha = jnp.exp(m_old - m_new)
            p = jnp.exp(s - m_new)
            if masked:
                p = jnp.where(allowed, p, 0.0)
            l_sc[h] = alpha * l_sc[h] + jnp.sum(p, axis=1, keepdims=True)
            pv = lax.dot_general(p.astype(jnp.bfloat16), v, (((1,), (0,)), ((), ())),
                                 preferred_element_type=jnp.float32)
            acc_sc[h] = alpha * acc_sc[h] + pv
            m_sc[h] = m_new

    @pl.when((blk <= hi) & full)
    def _():
        step(False)

    @pl.when((blk <= hi) & jnp.logical_not(full))
    def _():
        step(True)

    @pl.when(j == steps - 1)
    def _():
        for h in range(heads):
            o_ref[:, h * DH:(h + 1) * DH] = (acc_sc[h] / l_sc[h]).astype(o_ref.dtype)


def attend(bounds, query_rows, kv, query_doc, query_pos, factor, key_doc, steps, bk):
    rows, width = query_rows.shape
    heads = width // DH

    def kv_map(j, b):
        return (jnp.minimum(b[0] + j, b[1]), 0)

    def kdoc_map(j, b):
        return (0, jnp.minimum(b[0] + j, b[1]))

    whole = lambda j, b: (0, 0)
    return pl.pallas_call(
        functools.partial(flash_kernel, heads=heads, bk=bk, steps=steps),
        out_shape=jax.ShapeDtypeStruct((rows, width), jnp.bfloat16),
        grid_spec=pltpu.PrefetchScalarGridSpec(
            num_scalar_prefetch=1,
            grid=(steps,),
            in_specs=[
                pl.BlockSpec((rows, width), whole),
                pl.BlockSpec((bk, 2 * DH), kv_map),
                pl.BlockSpec((rows, 1), whole),
                pl.BlockSpec((rows, 1), whole),
                pl.BlockSpec((rows, 1), whole),
                pl.BlockSpec((1, bk), kdoc_map),
            ],
            out_specs=pl.BlockSpec((rows, width), whole),
            scratch_shapes=[
                pltpu.VMEM((heads, rows, 1), jnp.float32),
                pltpu.VMEM((heads, rows, 1), jnp.float32),
                pltpu.VMEM((heads, rows, DH), jnp.float32),
            ],
        ),
        compiler_params=pltpu.CompilerParams(dimension_semantics=("arbitrary",)),
    )(bounds, query_rows, kv, query_doc, query_pos, factor, key_doc)


def body(queries, keys, values, doc_lengths):
    query_rows = queries[0]
    key_rows = keys[0]
    value_rows = values[0]
    lengths = doc_lengths[0]
    rows = query_rows.shape[0]
    cycle = lax.axis_size("ctx")
    count = rows * cycle
    base_len = count // 16
    position = lax.axis_index("ctx")
    first = position * rows
    ends = jnp.cumsum(lengths)
    starts = ends - lengths
    query_pos = first + jnp.arange(rows, dtype=jnp.int32)
    query_doc = doc_of(query_pos, ends)
    lookup = query_doc[:, None] == jnp.arange(DOCS, dtype=jnp.int32)[None, :]
    query_len = jnp.sum(jnp.where(lookup, lengths[None, :], 0), axis=1).astype(jnp.float32)
    factor = jnp.maximum(1.0, jnp.log(query_len) / math.log(float(base_len))) * (
        1.0 / math.sqrt(DH)
    )
    bk = min(BK, count)
    span = max(
        (c * rows + rows - 1) // bk - max(0, c * rows - (MOST - 1)) // bk + 1
        for c in range(cycle)
    )
    first_doc = jnp.sum((first >= ends).astype(jnp.int32))
    lo = jnp.sum(jnp.where(jnp.arange(DOCS) == first_doc, starts, 0)) // bk
    hi = (first + rows - 1) // bk
    last_doc = jnp.sum((first + rows - 1 >= ends).astype(jnp.int32))
    block_first = jnp.minimum(lo + jnp.arange(span, dtype=jnp.int32), hi) * bk
    block_last = block_first + bk - 1
    full = (
        (doc_of(block_first, ends) == first_doc)
        & (doc_of(block_last, ends) == first_doc)
        & (last_doc == first_doc)
        & (block_last <= first)
    )
    bounds = jnp.concatenate([jnp.stack([lo, hi]), full.astype(jnp.int32)]).astype(jnp.int32)
    kv_rows = jnp.concatenate([key_rows, value_rows], axis=1)
    kv = lax.all_gather(kv_rows, "ctx", axis=0, tiled=True)
    key_doc = doc_of(jnp.arange(count, dtype=jnp.int32), ends)[None, :]
    result = attend(
        bounds, query_rows, kv, query_doc[:, None], query_pos[:, None], factor[:, None],
        key_doc, span, bk,
    )
    own = lax.all_to_all(result, "mp", split_axis=0, concat_axis=1, tiled=True)
    moved = from_behind(own, "section", 1)
    return (own[None], moved[None])


def solution(mesh):
    return jax.shard_map(
        body,
        mesh=mesh,
        in_specs=(
            P("section", "ctx", "mp"),
            P("section", "ctx", "mp"),
            P("section", "ctx", "mp"),
            P("section", None),
        ),
        out_specs=(P("section", ("ctx", "mp"), None), P("section", ("ctx", "mp"), None)),
        check_vma=False,
    )
```

```python
import functools
import math

import jax
import jax.numpy as jnp
from jax import lax
from jax.experimental import pallas as pl
from jax.experimental.pallas import tpu as pltpu
from jax.sharding import PartitionSpec as P

DH = 128
DOCS = 16
MOST = 4096
BK = 512


def doc_of(positions, ends):
    return jnp.sum((positions[:, None] >= ends[None, :]).astype(jnp.int32), axis=1)


def flash_kernel(bounds_ref, qt_ref, kv_ref, qdoc_ref, qpos_ref, fac_ref, kdoc_ref,
                 o_ref, m_sc, l_sc, acc_sc, *, heads, rows, bk, steps):
    j = pl.program_id(0)
    lo = bounds_ref[0]
    hi = bounds_ref[1]

    @pl.when(j == 0)
    def _():
        m_sc[...] = jnp.full(m_sc.shape, -1e30, jnp.float32)
        l_sc[...] = jnp.zeros(l_sc.shape, jnp.float32)
        acc_sc[...] = jnp.zeros(acc_sc.shape, jnp.float32)

    blk = lo + j
    full = bounds_ref[2 + j] == 1

    def step(masked):
        k = kv_ref[:, :DH]
        vt = kv_ref[:, DH:].T
        if masked:
            kpos = blk * bk + lax.broadcasted_iota(jnp.int32, (bk, 1), 0)
            allowed = (kdoc_ref[...] == qdoc_ref[...]) & (kpos <= qpos_ref[...])
        fac = fac_ref[...]
        for h in range(heads):
            cols = slice(h * rows, (h + 1) * rows)
            s = jnp.dot(k, qt_ref[h], preferred_element_type=jnp.float32)
            s = s * fac
            if masked:
                s = jnp.where(allowed, s, -1e30)
            m_old = m_sc[h]
            m_new = jnp.maximum(m_old, jnp.max(s, axis=0, keepdims=True))
            alpha = jnp.exp(m_old - m_new)
            p = jnp.exp(s - m_new)
            if masked:
                p = jnp.where(allowed, p, 0.0)
            l_sc[h] = alpha * l_sc[h] + jnp.sum(p, axis=0, keepdims=True)
            pv = jnp.dot(vt, p.astype(jnp.bfloat16), preferred_element_type=jnp.float32)
            acc_sc[h] = alpha * acc_sc[h] + pv
            m_sc[h] = m_new

    @pl.when((blk <= hi) & full)
    def _():
        step(False)

    @pl.when((blk <= hi) & jnp.logical_not(full))
    def _():
        step(True)

    @pl.when(j == steps - 1)
    def _():
        for h in range(heads):
            cols = slice(h * rows, (h + 1) * rows)
            o_ref[:, h * DH:(h + 1) * DH] = (acc_sc[h] / l_sc[h]).T.astype(o_ref.dtype)


def attend(bounds, query_rows, kv, query_doc, query_pos, factor, key_doc, steps, bk):
    rows, width = query_rows.shape
    heads = width // DH
    qt = query_rows.reshape(rows, heads, DH).transpose(1, 2, 0)

    def kv_map(j, b):
        return (jnp.minimum(b[0] + j, b[1]), 0)

    whole = lambda j, b: (0, 0)
    return pl.pallas_call(
        functools.partial(flash_kernel, heads=heads, rows=rows, bk=bk, steps=steps),
        out_shape=jax.ShapeDtypeStruct((rows, width), jnp.bfloat16),
        grid_spec=pltpu.PrefetchScalarGridSpec(
            num_scalar_prefetch=1,
            grid=(steps,),
            in_specs=[
                pl.BlockSpec((heads, DH, rows), lambda j, b: (0, 0, 0)),
                pl.BlockSpec((bk, 2 * DH), kv_map),
                pl.BlockSpec((1, rows), whole),
                pl.BlockSpec((1, rows), whole),
                pl.BlockSpec((1, rows), whole),
                pl.BlockSpec((bk, 1), kv_map),
            ],
            out_specs=pl.BlockSpec((rows, width), whole),
            scratch_shapes=[
                pltpu.VMEM((heads, 1, rows), jnp.float32),
                pltpu.VMEM((heads, 1, rows), jnp.float32),
                pltpu.VMEM((heads, DH, rows), jnp.float32),
            ],
        ),
        compiler_params=pltpu.CompilerParams(dimension_semantics=("arbitrary",)),
    )(bounds, qt, kv, query_doc.reshape(1, rows), query_pos.reshape(1, rows),
      factor.reshape(1, rows), key_doc.reshape(-1, 1))


def body(queries, keys, values, doc_lengths):
    query_rows = queries[0]
    key_rows = keys[0]
    value_rows = values[0]
    lengths = doc_lengths[0]
    rows = query_rows.shape[0]
    cycle = lax.axis_size("ctx")
    count = rows * cycle
    base_len = count // 16
    position = lax.axis_index("ctx")
    first = position * rows
    ends = jnp.cumsum(lengths)
    starts = ends - lengths
    query_pos = first + jnp.arange(rows, dtype=jnp.int32)
    query_doc = doc_of(query_pos, ends)
    lookup = query_doc[:, None] == jnp.arange(DOCS, dtype=jnp.int32)[None, :]
    query_len = jnp.sum(jnp.where(lookup, lengths[None, :], 0), axis=1).astype(jnp.float32)
    factor = jnp.maximum(1.0, jnp.log(query_len) / math.log(float(base_len))) * (
        1.0 / math.sqrt(DH)
    )
    bk = min(BK, count)
    span = max(
        (c * rows + rows - 1) // bk - max(0, c * rows - (MOST - 1)) // bk + 1
        for c in range(cycle)
    )
    first_doc = jnp.sum((first >= ends).astype(jnp.int32))
    lo = jnp.sum(jnp.where(jnp.arange(DOCS) == first_doc, starts, 0)) // bk
    hi = (first + rows - 1) // bk
    last_doc = jnp.sum((first + rows - 1 >= ends).astype(jnp.int32))
    block_first = jnp.minimum(lo + jnp.arange(span, dtype=jnp.int32), hi) * bk
    block_last = block_first + bk - 1
    full = (
        (doc_of(block_first, ends) == first_doc)
        & (doc_of(block_last, ends) == first_doc)
        & (last_doc == first_doc)
        & (block_last <= first)
    )
    bounds = jnp.concatenate([jnp.stack([lo, hi]), full.astype(jnp.int32)]).astype(jnp.int32)
    kv_rows = jnp.concatenate([key_rows, value_rows], axis=1)
    kv = lax.all_gather(kv_rows, "ctx", axis=0, tiled=True)
    key_doc = doc_of(jnp.arange(count, dtype=jnp.int32), ends)[None, :]
    result = attend(
        bounds, query_rows, kv, query_doc[:, None], query_pos[:, None], factor[:, None],
        key_doc, span, bk,
    )
    share = lax.axis_size("mp")
    chunks = result.reshape(share, rows // share, result.shape[1])
    sections = lax.axis_size("section")
    got = lax.all_to_all(
        jnp.concatenate([chunks] * sections, axis=0), ("section", "mp"), 0, 0, tiled=False
    ).reshape(sections, share, rows // share, result.shape[1])
    here = lax.axis_index("section")
    behind = (here + sections - 1) % sections
    own = jnp.take(got, here, axis=0)
    moved = jnp.take(got, behind, axis=0)
    own = own.transpose(1, 0, 2).reshape(rows // share, share * result.shape[1])
    moved = moved.transpose(1, 0, 2).reshape(rows // share, share * result.shape[1])
    return (own[None], moved[None])


def solution(mesh):
    return jax.shard_map(
        body,
        mesh=mesh,
        in_specs=(
            P("section", "ctx", "mp"),
            P("section", "ctx", "mp"),
            P("section", "ctx", "mp"),
            P("section", None),
        ),
        out_specs=(P("section", ("ctx", "mp"), None), P("section", ("ctx", "mp"), None)),
        check_vma=False,
    )
```

```python
import functools
import math

import jax
import jax.numpy as jnp
from jax import lax
from jax.experimental import pallas as pl
from jax.experimental.pallas import tpu as pltpu
from jax.sharding import PartitionSpec as P

DH = 128
DOCS = 16
MOST = 4096
BK = 512


def doc_of(positions, ends):
    return jnp.sum((positions[:, None] >= ends[None, :]).astype(jnp.int32), axis=1)


def flash_kernel(bounds_ref, qt_ref, kv_ref, qdoc_ref, qpos_ref, fac_ref, kdoc_ref,
                 o_ref, m_sc, l_sc, acc_sc, *, heads, rows, bk, steps):
    j = pl.program_id(0)
    lo = bounds_ref[0]
    hi = bounds_ref[1]

    @pl.when(j == 0)
    def _():
        m_sc[...] = jnp.full(m_sc.shape, -1e30, jnp.float32)
        l_sc[...] = jnp.zeros(l_sc.shape, jnp.float32)
        acc_sc[...] = jnp.zeros(acc_sc.shape, jnp.float32)

    blk = lo + j
    full = bounds_ref[2 + j] == 1

    def step(masked):
        k = kv_ref[:, :DH]
        vt = kv_ref[:, DH:].T
        fac = jnp.concatenate([fac_ref[...]] * heads, axis=1)
        s = jnp.dot(k, qt_ref[...], preferred_element_type=jnp.float32)
        s = s * fac
        if masked:
            kpos = blk * bk + lax.broadcasted_iota(jnp.int32, (bk, 1), 0)
            allowed = (kdoc_ref[...] == qdoc_ref[...]) & (kpos <= qpos_ref[...])
            allowed = jnp.concatenate([allowed] * heads, axis=1)
            s = jnp.where(allowed, s, -1e30)
        m_old = m_sc[...]
        m_new = jnp.maximum(m_old, jnp.max(s, axis=0, keepdims=True))
        alpha = jnp.exp(m_old - m_new)
        p = jnp.exp(s - m_new)
        if masked:
            p = jnp.where(allowed, p, 0.0)
        l_sc[...] = alpha * l_sc[...] + jnp.sum(p, axis=0, keepdims=True)
        pv = jnp.dot(vt, p.astype(jnp.bfloat16), preferred_element_type=jnp.float32)
        acc_sc[...] = alpha * acc_sc[...] + pv
        m_sc[...] = m_new

    @pl.when((blk <= hi) & full)
    def _():
        step(False)

    @pl.when((blk <= hi) & jnp.logical_not(full))
    def _():
        step(True)

    @pl.when(j == steps - 1)
    def _():
        for h in range(heads):
            cols = slice(h * rows, (h + 1) * rows)
            o_ref[:, h * DH:(h + 1) * DH] = (acc_sc[:, cols] / l_sc[:, cols]).T.astype(o_ref.dtype)


def attend(bounds, query_rows, kv, query_doc, query_pos, factor, key_doc, steps, bk):
    rows, width = query_rows.shape
    heads = width // DH
    qt = query_rows.reshape(rows, heads, DH).transpose(2, 1, 0).reshape(DH, heads * rows)

    def kv_map(j, b):
        return (jnp.minimum(b[0] + j, b[1]), 0)

    whole = lambda j, b: (0, 0)
    return pl.pallas_call(
        functools.partial(flash_kernel, heads=heads, rows=rows, bk=bk, steps=steps),
        out_shape=jax.ShapeDtypeStruct((rows, width), jnp.bfloat16),
        grid_spec=pltpu.PrefetchScalarGridSpec(
            num_scalar_prefetch=1,
            grid=(steps,),
            in_specs=[
                pl.BlockSpec((DH, heads * rows), whole),
                pl.BlockSpec((bk, 2 * DH), kv_map),
                pl.BlockSpec((1, rows), whole),
                pl.BlockSpec((1, rows), whole),
                pl.BlockSpec((1, rows), whole),
                pl.BlockSpec((bk, 1), kv_map),
            ],
            out_specs=pl.BlockSpec((rows, width), whole),
            scratch_shapes=[
                pltpu.VMEM((1, heads * rows), jnp.float32),
                pltpu.VMEM((1, heads * rows), jnp.float32),
                pltpu.VMEM((DH, heads * rows), jnp.float32),
            ],
        ),
        compiler_params=pltpu.CompilerParams(dimension_semantics=("arbitrary",)),
    )(bounds, qt, kv, query_doc.reshape(1, rows), query_pos.reshape(1, rows),
      factor.reshape(1, rows), key_doc.reshape(-1, 1))


def body(queries, keys, values, doc_lengths):
    query_rows = queries[0]
    key_rows = keys[0]
    value_rows = values[0]
    lengths = doc_lengths[0]
    rows = query_rows.shape[0]
    cycle = lax.axis_size("ctx")
    count = rows * cycle
    base_len = count // 16
    position = lax.axis_index("ctx")
    first = position * rows
    ends = jnp.cumsum(lengths)
    starts = ends - lengths
    query_pos = first + jnp.arange(rows, dtype=jnp.int32)
    query_doc = doc_of(query_pos, ends)
    lookup = query_doc[:, None] == jnp.arange(DOCS, dtype=jnp.int32)[None, :]
    query_len = jnp.sum(jnp.where(lookup, lengths[None, :], 0), axis=1).astype(jnp.float32)
    factor = jnp.maximum(1.0, jnp.log(query_len) / math.log(float(base_len))) * (
        1.0 / math.sqrt(DH)
    )
    bk = min(BK, count)
    span = max(
        (c * rows + rows - 1) // bk - max(0, c * rows - (MOST - 1)) // bk + 1
        for c in range(cycle)
    )
    first_doc = jnp.sum((first >= ends).astype(jnp.int32))
    lo = jnp.sum(jnp.where(jnp.arange(DOCS) == first_doc, starts, 0)) // bk
    hi = (first + rows - 1) // bk
    last_doc = jnp.sum((first + rows - 1 >= ends).astype(jnp.int32))
    block_first = jnp.minimum(lo + jnp.arange(span, dtype=jnp.int32), hi) * bk
    block_last = block_first + bk - 1
    full = (
        (doc_of(block_first, ends) == first_doc)
        & (doc_of(block_last, ends) == first_doc)
        & (last_doc == first_doc)
        & (block_last <= first)
    )
    bounds = jnp.concatenate([jnp.stack([lo, hi]), full.astype(jnp.int32)]).astype(jnp.int32)
    kv_rows = jnp.concatenate([key_rows, value_rows], axis=1)
    kv = lax.all_gather(kv_rows, "ctx", axis=0, tiled=True)
    key_doc = doc_of(jnp.arange(count, dtype=jnp.int32), ends)[None, :]
    result = attend(
        bounds, query_rows, kv, query_doc[:, None], query_pos[:, None], factor[:, None],
        key_doc, span, bk,
    )
    share = lax.axis_size("mp")
    chunks = result.reshape(share, rows // share, result.shape[1])
    sections = lax.axis_size("section")
    got = lax.all_to_all(
        jnp.concatenate([chunks] * sections, axis=0), ("section", "mp"), 0, 0, tiled=False
    ).reshape(sections, share, rows // share, result.shape[1])
    here = lax.axis_index("section")
    behind = (here + sections - 1) % sections
    own = jnp.take(got, here, axis=0)
    moved = jnp.take(got, behind, axis=0)
    own = own.transpose(1, 0, 2).reshape(rows // share, share * result.shape[1])
    moved = moved.transpose(1, 0, 2).reshape(rows // share, share * result.shape[1])
    return (own[None], moved[None])


def solution(mesh):
    return jax.shard_map(
        body,
        mesh=mesh,
        in_specs=(
            P("section", "ctx", "mp"),
            P("section", "ctx", "mp"),
            P("section", "ctx", "mp"),
            P("section", None),
        ),
        out_specs=(P("section", ("ctx", "mp"), None), P("section", ("ctx", "mp"), None)),
        check_vma=False,
    )
```

```python
import functools
import math

import jax
import jax.numpy as jnp
from jax import lax
from jax.experimental import pallas as pl
from jax.experimental.pallas import tpu as pltpu
from jax.sharding import PartitionSpec as P

DH = 128
DOCS = 16
MOST = 4096
BK = 512


def doc_of(positions, ends):
    return jnp.sum((positions[:, None] >= ends[None, :]).astype(jnp.int32), axis=1)


def flash_kernel(bounds_ref, qt_ref, kv_ref, qdoc_ref, qpos_ref, fac_ref, kdoc_ref,
                 o_ref, m_sc, l_sc, acc_sc, *, heads, rows, bk, steps, copies):
    j = pl.program_id(0)
    lo = bounds_ref[0]
    hi = bounds_ref[1]

    @pl.when(j == 0)
    def _():
        m_sc[...] = jnp.full(m_sc.shape, -1e30, jnp.float32)
        l_sc[...] = jnp.zeros(l_sc.shape, jnp.float32)
        acc_sc[...] = jnp.zeros(acc_sc.shape, jnp.float32)

    blk = lo + j
    full = bounds_ref[2 + j] == 1

    def step(masked):
        k = kv_ref[:, :DH]
        vt = kv_ref[:, DH:].T
        fac = jnp.concatenate([fac_ref[...]] * heads, axis=1)
        s = jnp.dot(k, qt_ref[...], preferred_element_type=jnp.float32)
        s = s * fac
        if masked:
            kpos = blk * bk + lax.broadcasted_iota(jnp.int32, (bk, 1), 0)
            allowed = (kdoc_ref[...] == qdoc_ref[...]) & (kpos <= qpos_ref[...])
            allowed = jnp.concatenate([allowed] * heads, axis=1)
            s = jnp.where(allowed, s, -1e30)
        m_old = m_sc[...]
        m_new = jnp.maximum(m_old, jnp.max(s, axis=0, keepdims=True))
        alpha = jnp.exp(m_old - m_new)
        p = jnp.exp(s - m_new)
        if masked:
            p = jnp.where(allowed, p, 0.0)
        l_sc[...] = alpha * l_sc[...] + jnp.sum(p, axis=0, keepdims=True)
        pv = jnp.dot(vt, p.astype(jnp.bfloat16), preferred_element_type=jnp.float32)
        acc_sc[...] = alpha * acc_sc[...] + pv
        m_sc[...] = m_new

    @pl.when((blk <= hi) & full)
    def _():
        step(False)

    @pl.when((blk <= hi) & jnp.logical_not(full))
    def _():
        step(True)

    @pl.when(j == steps - 1)
    def _():
        for h in range(heads):
            cols = slice(h * rows, (h + 1) * rows)
            out = (acc_sc[:, cols] / l_sc[:, cols]).T.astype(o_ref.dtype)
            for c in range(copies):
                o_ref[c, :, h * DH:(h + 1) * DH] = out


def attend(bounds, query_rows, kv, query_doc, query_pos, factor, key_doc, steps, bk, copies):
    rows, width = query_rows.shape
    heads = width // DH
    qt = query_rows.reshape(rows, heads, DH).transpose(2, 1, 0).reshape(DH, heads * rows)

    def kv_map(j, b):
        return (jnp.minimum(b[0] + j, b[1]), 0)

    whole = lambda j, b: (0, 0)
    return pl.pallas_call(
        functools.partial(flash_kernel, heads=heads, rows=rows, bk=bk, steps=steps,
                          copies=copies),
        out_shape=jax.ShapeDtypeStruct((copies, rows, width), jnp.bfloat16),
        grid_spec=pltpu.PrefetchScalarGridSpec(
            num_scalar_prefetch=1,
            grid=(steps,),
            in_specs=[
                pl.BlockSpec((DH, heads * rows), whole),
                pl.BlockSpec((bk, 2 * DH), kv_map),
                pl.BlockSpec((1, rows), whole),
                pl.BlockSpec((1, rows), whole),
                pl.BlockSpec((1, rows), whole),
                pl.BlockSpec((bk, 1), kv_map),
            ],
            out_specs=pl.BlockSpec((copies, rows, width), lambda j, b: (0, 0, 0)),
            scratch_shapes=[
                pltpu.VMEM((1, heads * rows), jnp.float32),
                pltpu.VMEM((1, heads * rows), jnp.float32),
                pltpu.VMEM((DH, heads * rows), jnp.float32),
            ],
        ),
        compiler_params=pltpu.CompilerParams(dimension_semantics=("arbitrary",)),
    )(bounds, qt, kv, query_doc.reshape(1, rows), query_pos.reshape(1, rows),
      factor.reshape(1, rows), key_doc.reshape(-1, 1))


def body(queries, keys, values, doc_lengths):
    query_rows = queries[0]
    key_rows = keys[0]
    value_rows = values[0]
    lengths = doc_lengths[0]
    rows = query_rows.shape[0]
    cycle = lax.axis_size("ctx")
    count = rows * cycle
    base_len = count // 16
    position = lax.axis_index("ctx")
    first = position * rows
    ends = jnp.cumsum(lengths)
    starts = ends - lengths
    query_pos = first + jnp.arange(rows, dtype=jnp.int32)
    query_doc = doc_of(query_pos, ends)
    lookup = query_doc[:, None] == jnp.arange(DOCS, dtype=jnp.int32)[None, :]
    query_len = jnp.sum(jnp.where(lookup, lengths[None, :], 0), axis=1).astype(jnp.float32)
    factor = jnp.maximum(1.0, jnp.log(query_len) / math.log(float(base_len))) * (
        1.0 / math.sqrt(DH)
    )
    bk = min(BK, count)
    span = max(
        (c * rows + rows - 1) // bk - max(0, c * rows - (MOST - 1)) // bk + 1
        for c in range(cycle)
    )
    first_doc = jnp.sum((first >= ends).astype(jnp.int32))
    lo = jnp.sum(jnp.where(jnp.arange(DOCS) == first_doc, starts, 0)) // bk
    hi = (first + rows - 1) // bk
    last_doc = jnp.sum((first + rows - 1 >= ends).astype(jnp.int32))
    block_first = jnp.minimum(lo + jnp.arange(span, dtype=jnp.int32), hi) * bk
    block_last = block_first + bk - 1
    full = (
        (doc_of(block_first, ends) == first_doc)
        & (doc_of(block_last, ends) == first_doc)
        & (last_doc == first_doc)
        & (block_last <= first)
    )
    bounds = jnp.concatenate([jnp.stack([lo, hi]), full.astype(jnp.int32)]).astype(jnp.int32)
    kv_rows = jnp.concatenate([key_rows, value_rows], axis=1)
    kv = lax.all_gather(kv_rows, "ctx", axis=0, tiled=True)
    key_doc = doc_of(jnp.arange(count, dtype=jnp.int32), ends)[None, :]
    sections = lax.axis_size("section")
    result = attend(
        bounds, query_rows, kv, query_doc[:, None], query_pos[:, None], factor[:, None],
        key_doc, span, bk, sections,
    )
    share = lax.axis_size("mp")
    width = result.shape[2]
    got = lax.all_to_all(
        result.reshape(sections * rows, width), ("section", "mp"), 0, 1, tiled=True
    )
    here = lax.axis_index("section")
    behind = (here + sections - 1) % sections
    span_cols = share * width
    own = lax.dynamic_slice_in_dim(got, here * span_cols, span_cols, axis=1)
    moved = lax.dynamic_slice_in_dim(got, behind * span_cols, span_cols, axis=1)
    return (own[None], moved[None])


def solution(mesh):
    return jax.shard_map(
        body,
        mesh=mesh,
        in_specs=(
            P("section", "ctx", "mp"),
            P("section", "ctx", "mp"),
            P("section", "ctx", "mp"),
            P("section", None),
        ),
        out_specs=(P("section", ("ctx", "mp"), None), P("section", ("ctx", "mp"), None)),
        check_vma=False,
    )
```

```python
import functools
import math

import jax
import jax.numpy as jnp
from jax import lax
from jax.experimental import pallas as pl
from jax.experimental.pallas import tpu as pltpu
from jax.sharding import PartitionSpec as P

DH = 128
DOCS = 16
MOST = 4096
BK = 512


def doc_of(positions, ends):
    return jnp.sum((positions[:, None] >= ends[None, :]).astype(jnp.int32), axis=1)


def flash_kernel(bounds_ref, qt_ref, k_ref, v_ref, qdoc_ref, qpos_ref, fac_ref, kdoc_ref,
                 o_ref, m_sc, l_sc, acc_sc, *, heads, rows, bk, steps, copies):
    j = pl.program_id(0)
    lo = bounds_ref[0]
    hi = bounds_ref[1]

    @pl.when(j == 0)
    def _():
        m_sc[...] = jnp.full(m_sc.shape, -1e30, jnp.float32)
        l_sc[...] = jnp.zeros(l_sc.shape, jnp.float32)
        acc_sc[...] = jnp.zeros(acc_sc.shape, jnp.float32)

    blk = lo + j
    full = bounds_ref[2 + j] == 1

    def step(masked):
        k = k_ref[...].reshape(bk, DH)
        vt = v_ref[...].reshape(bk, DH).T
        fac = jnp.concatenate([fac_ref[...]] * heads, axis=1)
        s = jnp.dot(k, qt_ref[...], preferred_element_type=jnp.float32)
        s = s * fac
        if masked:
            kpos = blk * bk + lax.broadcasted_iota(jnp.int32, (bk, 1), 0)
            allowed = (kdoc_ref[...] == qdoc_ref[...]) & (kpos <= qpos_ref[...])
            allowed = jnp.concatenate([allowed] * heads, axis=1)
            s = jnp.where(allowed, s, -1e30)
        m_old = m_sc[...]
        m_new = jnp.maximum(m_old, jnp.max(s, axis=0, keepdims=True))
        alpha = jnp.exp(m_old - m_new)
        p = jnp.exp(s - m_new)
        if masked:
            p = jnp.where(allowed, p, 0.0)
        l_sc[...] = alpha * l_sc[...] + jnp.sum(p, axis=0, keepdims=True)
        pv = jnp.dot(vt, p.astype(jnp.bfloat16), preferred_element_type=jnp.float32)
        acc_sc[...] = alpha * acc_sc[...] + pv
        m_sc[...] = m_new

    @pl.when((blk <= hi) & full)
    def _():
        step(False)

    @pl.when((blk <= hi) & jnp.logical_not(full))
    def _():
        step(True)

    @pl.when(j == steps - 1)
    def _():
        for h in range(heads):
            cols = slice(h * rows, (h + 1) * rows)
            out = (acc_sc[:, cols] / l_sc[:, cols]).T.astype(o_ref.dtype)
            for c in range(copies):
                o_ref[c, :, h * DH:(h + 1) * DH] = out


def attend(bounds, query_rows, kv, query_doc, query_pos, factor, key_doc, steps, bk, copies):
    rows, width = query_rows.shape
    heads = width // DH
    qt = query_rows.reshape(rows, heads, DH).transpose(2, 1, 0).reshape(DH, heads * rows)

    def kv_map(j, b):
        return (jnp.minimum(b[0] + j, b[1]), 0)

    def k_map(j, b):
        return (jnp.minimum(b[0] + j, b[1]), 0, 0, 0)

    def v_map(j, b):
        return (jnp.minimum(b[0] + j, b[1]), 1, 0, 0)

    per = kv.shape[2]

    whole = lambda j, b: (0, 0)
    return pl.pallas_call(
        functools.partial(flash_kernel, heads=heads, rows=rows, bk=bk, steps=steps,
                          copies=copies),
        out_shape=jax.ShapeDtypeStruct((copies, rows, width), jnp.bfloat16),
        grid_spec=pltpu.PrefetchScalarGridSpec(
            num_scalar_prefetch=1,
            grid=(steps,),
            in_specs=[
                pl.BlockSpec((DH, heads * rows), whole),
                pl.BlockSpec((bk // per, None, per, DH), k_map),
                pl.BlockSpec((bk // per, None, per, DH), v_map),
                pl.BlockSpec((1, rows), whole),
                pl.BlockSpec((1, rows), whole),
                pl.BlockSpec((1, rows), whole),
                pl.BlockSpec((bk, 1), kv_map),
            ],
            out_specs=pl.BlockSpec((copies, rows, width), lambda j, b: (0, 0, 0)),
            scratch_shapes=[
                pltpu.VMEM((1, heads * rows), jnp.float32),
                pltpu.VMEM((1, heads * rows), jnp.float32),
                pltpu.VMEM((DH, heads * rows), jnp.float32),
            ],
        ),
        compiler_params=pltpu.CompilerParams(dimension_semantics=("arbitrary",)),
    )(bounds, qt, kv, kv, query_doc.reshape(1, rows), query_pos.reshape(1, rows),
      factor.reshape(1, rows), key_doc.reshape(-1, 1))


def body(queries, keys, values, doc_lengths):
    query_rows = queries[0]
    key_rows = keys[0]
    value_rows = values[0]
    lengths = doc_lengths[0]
    rows = query_rows.shape[0]
    cycle = lax.axis_size("ctx")
    count = rows * cycle
    base_len = count // 16
    position = lax.axis_index("ctx")
    first = position * rows
    ends = jnp.cumsum(lengths)
    starts = ends - lengths
    query_pos = first + jnp.arange(rows, dtype=jnp.int32)
    query_doc = doc_of(query_pos, ends)
    lookup = query_doc[:, None] == jnp.arange(DOCS, dtype=jnp.int32)[None, :]
    query_len = jnp.sum(jnp.where(lookup, lengths[None, :], 0), axis=1).astype(jnp.float32)
    factor = jnp.maximum(1.0, jnp.log(query_len) / math.log(float(base_len))) * (
        1.0 / math.sqrt(DH)
    )
    bk = min(BK, count)
    span = max(
        (c * rows + rows - 1) // bk - max(0, c * rows - (MOST - 1)) // bk + 1
        for c in range(cycle)
    )
    first_doc = jnp.sum((first >= ends).astype(jnp.int32))
    lo = jnp.sum(jnp.where(jnp.arange(DOCS) == first_doc, starts, 0)) // bk
    hi = (first + rows - 1) // bk
    last_doc = jnp.sum((first + rows - 1 >= ends).astype(jnp.int32))
    block_first = jnp.minimum(lo + jnp.arange(span, dtype=jnp.int32), hi) * bk
    block_last = block_first + bk - 1
    full = (
        (doc_of(block_first, ends) == first_doc)
        & (doc_of(block_last, ends) == first_doc)
        & (last_doc == first_doc)
        & (block_last <= first)
    )
    bounds = jnp.concatenate([jnp.stack([lo, hi]), full.astype(jnp.int32)]).astype(jnp.int32)
    kv_rows = jnp.concatenate([key_rows, value_rows], axis=0)
    kv = lax.all_gather(kv_rows, "ctx", axis=0, tiled=False).reshape(cycle, 2, rows, DH)
    key_doc = doc_of(jnp.arange(count, dtype=jnp.int32), ends)[None, :]
    sections = lax.axis_size("section")
    result = attend(
        bounds, query_rows, kv, query_doc[:, None], query_pos[:, None], factor[:, None],
        key_doc, span, bk, sections,
    )
    share = lax.axis_size("mp")
    width = result.shape[2]
    got = lax.all_to_all(
        result.reshape(sections * rows, width), ("section", "mp"), 0, 1, tiled=True
    )
    here = lax.axis_index("section")
    behind = (here + sections - 1) % sections
    span_cols = share * width
    own = lax.dynamic_slice_in_dim(got, here * span_cols, span_cols, axis=1)
    moved = lax.dynamic_slice_in_dim(got, behind * span_cols, span_cols, axis=1)
    return (own[None], moved[None])


def solution(mesh):
    return jax.shard_map(
        body,
        mesh=mesh,
        in_specs=(
            P("section", "ctx", "mp"),
            P("section", "ctx", "mp"),
            P("section", "ctx", "mp"),
            P("section", None),
        ),
        out_specs=(P("section", ("ctx", "mp"), None), P("section", ("ctx", "mp"), None)),
        check_vma=False,
    )
```

```python
import functools
import math

import jax
import jax.numpy as jnp
from jax import lax
from jax.experimental import pallas as pl
from jax.experimental.pallas import tpu as pltpu
from jax.sharding import PartitionSpec as P

DH = 128
LOG2E = 1.4426950408889634
DOCS = 16
MOST = 4096
BK = 512


def doc_of(positions, ends):
    return jnp.sum((positions[:, None] >= ends[None, :]).astype(jnp.int32), axis=1)


def flash_kernel(bounds_ref, qt_ref, kv_ref, qdoc_ref, qpos_ref, fac_ref, kdoc_ref,
                 o_ref, m_sc, l_sc, acc_sc, *, heads, rows, bk, steps, copies):
    j = pl.program_id(0)
    lo = bounds_ref[0]
    hi = bounds_ref[1]

    @pl.when(j == 0)
    def _():
        m_sc[...] = jnp.full(m_sc.shape, -1e30, jnp.float32)
        l_sc[...] = jnp.zeros(l_sc.shape, jnp.float32)
        acc_sc[...] = jnp.zeros(acc_sc.shape, jnp.float32)

    blk = lo + j
    full = bounds_ref[2 + j] == 1

    def step(masked):
        k = kv_ref[:, :DH]
        vt = kv_ref[:, DH:].T
        fac = jnp.concatenate([fac_ref[...]] * heads, axis=1)
        s = jnp.dot(k, qt_ref[...], preferred_element_type=jnp.float32)
        s = s * (fac * LOG2E)
        if masked:
            kpos = blk * bk + lax.broadcasted_iota(jnp.int32, (bk, 1), 0)
            allowed = (kdoc_ref[...] == qdoc_ref[...]) & (kpos <= qpos_ref[...])
            allowed = jnp.concatenate([allowed] * heads, axis=1)
            s = jnp.where(allowed, s, -1e30)
        m_old = m_sc[...]
        m_new = jnp.maximum(m_old, jnp.max(s, axis=0, keepdims=True))
        alpha = jnp.exp2(m_old - m_new)
        p = jnp.exp2(s - m_new)
        if masked:
            p = jnp.where(allowed, p, 0.0)
        l_sc[...] = alpha * l_sc[...] + jnp.sum(p, axis=0, keepdims=True)
        pv = jnp.dot(vt, p.astype(jnp.bfloat16), preferred_element_type=jnp.float32)
        acc_sc[...] = alpha * acc_sc[...] + pv
        m_sc[...] = m_new

    @pl.when((blk <= hi) & full)
    def _():
        step(False)

    @pl.when((blk <= hi) & jnp.logical_not(full))
    def _():
        step(True)

    @pl.when(j == steps - 1)
    def _():
        for h in range(heads):
            cols = slice(h * rows, (h + 1) * rows)
            out = (acc_sc[:, cols] / l_sc[:, cols]).T.astype(o_ref.dtype)
            for c in range(copies):
                o_ref[c, :, h * DH:(h + 1) * DH] = out


def attend(bounds, query_rows, kv, query_doc, query_pos, factor, key_doc, steps, bk, copies):
    rows, width = query_rows.shape
    heads = width // DH
    qt = query_rows.reshape(rows, heads, DH).transpose(2, 1, 0).reshape(DH, heads * rows)

    def kv_map(j, b):
        return (jnp.minimum(b[0] + j, b[1]), 0)

    whole = lambda j, b: (0, 0)
    return pl.pallas_call(
        functools.partial(flash_kernel, heads=heads, rows=rows, bk=bk, steps=steps,
                          copies=copies),
        out_shape=jax.ShapeDtypeStruct((copies, rows, width), jnp.bfloat16),
        grid_spec=pltpu.PrefetchScalarGridSpec(
            num_scalar_prefetch=1,
            grid=(steps,),
            in_specs=[
                pl.BlockSpec((DH, heads * rows), whole),
                pl.BlockSpec((bk, 2 * DH), kv_map),
                pl.BlockSpec((1, rows), whole),
                pl.BlockSpec((1, rows), whole),
                pl.BlockSpec((1, rows), whole),
                pl.BlockSpec((bk, 1), kv_map),
            ],
            out_specs=pl.BlockSpec((copies, rows, width), lambda j, b: (0, 0, 0)),
            scratch_shapes=[
                pltpu.VMEM((1, heads * rows), jnp.float32),
                pltpu.VMEM((1, heads * rows), jnp.float32),
                pltpu.VMEM((DH, heads * rows), jnp.float32),
            ],
        ),
        compiler_params=pltpu.CompilerParams(dimension_semantics=("arbitrary",)),
    )(bounds, qt, kv, query_doc.reshape(1, rows), query_pos.reshape(1, rows),
      factor.reshape(1, rows), key_doc.reshape(-1, 1))


def body(queries, keys, values, doc_lengths):
    query_rows = queries[0]
    key_rows = keys[0]
    value_rows = values[0]
    lengths = doc_lengths[0]
    rows = query_rows.shape[0]
    cycle = lax.axis_size("ctx")
    count = rows * cycle
    base_len = count // 16
    position = lax.axis_index("ctx")
    first = position * rows
    ends = jnp.cumsum(lengths)
    starts = ends - lengths
    query_pos = first + jnp.arange(rows, dtype=jnp.int32)
    query_doc = doc_of(query_pos, ends)
    lookup = query_doc[:, None] == jnp.arange(DOCS, dtype=jnp.int32)[None, :]
    query_len = jnp.sum(jnp.where(lookup, lengths[None, :], 0), axis=1).astype(jnp.float32)
    factor = jnp.maximum(1.0, jnp.log(query_len) / math.log(float(base_len))) * (
        1.0 / math.sqrt(DH)
    )
    bk = min(BK, count)
    span = max(
        (c * rows + rows - 1) // bk - max(0, c * rows - (MOST - 1)) // bk + 1
        for c in range(cycle)
    )
    first_doc = jnp.sum((first >= ends).astype(jnp.int32))
    lo = jnp.sum(jnp.where(jnp.arange(DOCS) == first_doc, starts, 0)) // bk
    hi = (first + rows - 1) // bk
    last_doc = jnp.sum((first + rows - 1 >= ends).astype(jnp.int32))
    block_first = jnp.minimum(lo + jnp.arange(span, dtype=jnp.int32), hi) * bk
    block_last = block_first + bk - 1
    full = (
        (doc_of(block_first, ends) == first_doc)
        & (doc_of(block_last, ends) == first_doc)
        & (last_doc == first_doc)
        & (block_last <= first)
    )
    bounds = jnp.concatenate([jnp.stack([lo, hi]), full.astype(jnp.int32)]).astype(jnp.int32)
    kv_rows = jnp.concatenate([key_rows, value_rows], axis=1)
    kv = lax.all_gather(kv_rows, "ctx", axis=0, tiled=True)
    key_doc = doc_of(jnp.arange(count, dtype=jnp.int32), ends)[None, :]
    sections = lax.axis_size("section")
    result = attend(
        bounds, query_rows, kv, query_doc[:, None], query_pos[:, None], factor[:, None],
        key_doc, span, bk, sections,
    )
    share = lax.axis_size("mp")
    width = result.shape[2]
    got = lax.all_to_all(
        result.reshape(sections * rows, width), ("section", "mp"), 0, 1, tiled=True
    )
    here = lax.axis_index("section")
    behind = (here + sections - 1) % sections
    span_cols = share * width
    own = lax.dynamic_slice_in_dim(got, here * span_cols, span_cols, axis=1)
    moved = lax.dynamic_slice_in_dim(got, behind * span_cols, span_cols, axis=1)
    return (own[None], moved[None])


def solution(mesh):
    return jax.shard_map(
        body,
        mesh=mesh,
        in_specs=(
            P("section", "ctx", "mp"),
            P("section", "ctx", "mp"),
            P("section", "ctx", "mp"),
            P("section", None),
        ),
        out_specs=(P("section", ("ctx", "mp"), None), P("section", ("ctx", "mp"), None)),
        check_vma=False,
    )
```

```python
import functools
import math

import jax
import jax.numpy as jnp
from jax import lax
from jax.experimental import pallas as pl
from jax.experimental.pallas import tpu as pltpu
from jax.sharding import PartitionSpec as P

DH = 128
LOG2E = 1.4426950408889634
DOCS = 16
MOST = 4096
BK = 512


def doc_of(positions, ends):
    return jnp.sum((positions[:, None] >= ends[None, :]).astype(jnp.int32), axis=1)


def update(k, vt, qt, fac, allowed, m_ref, l_ref, acc_ref):
    s = jnp.dot(k, qt, preferred_element_type=jnp.float32)
    s = s * (fac * LOG2E)
    if allowed is not None:
        s = jnp.where(allowed, s, -1e30)
    m_old = m_ref[...]
    m_new = jnp.maximum(m_old, jnp.max(s, axis=0, keepdims=True))
    alpha = jnp.exp2(m_old - m_new)
    p = jnp.exp2(s - m_new)
    if allowed is not None:
        p = jnp.where(allowed, p, 0.0)
    l_ref[...] = alpha * l_ref[...] + jnp.sum(p, axis=0, keepdims=True)
    pv = jnp.dot(vt, p.astype(jnp.bfloat16), preferred_element_type=jnp.float32)
    acc_ref[...] = alpha * acc_ref[...] + pv
    m_ref[...] = m_new


def local_kernel(qt_ref, kv_ref, qdoc_ref, qpos_ref, fac_ref, kdoc_ref, kpos_ref,
                 m_ref, l_ref, acc_ref, *, heads):
    m_ref[...] = jnp.full(m_ref.shape, -1e30, jnp.float32)
    l_ref[...] = jnp.zeros(l_ref.shape, jnp.float32)
    acc_ref[...] = jnp.zeros(acc_ref.shape, jnp.float32)
    allowed = (kdoc_ref[...] == qdoc_ref[...]) & (kpos_ref[...] <= qpos_ref[...])
    allowed = jnp.concatenate([allowed] * heads, axis=1)
    fac = jnp.concatenate([fac_ref[...]] * heads, axis=1)
    update(kv_ref[:, :DH], kv_ref[:, DH:].T, qt_ref[...], fac, allowed, m_ref, l_ref, acc_ref)


def far_kernel(plan_ref, qt_ref, kv_ref, qdoc_ref, fac_ref, kdoc_ref, m0_ref, l0_ref, acc0_ref,
               o_ref, m_sc, l_sc, acc_sc, *, heads, rows, bk, steps, copies):
    j = pl.program_id(0)
    start = plan_ref[j]
    limit = plan_ref[steps + j]
    mode = plan_ref[2 * steps + j]

    @pl.when(j == 0)
    def _():
        m_sc[...] = m0_ref[...]
        l_sc[...] = l0_ref[...]
        acc_sc[...] = acc0_ref[...]

    def step(masked):
        fac = jnp.concatenate([fac_ref[...]] * heads, axis=1)
        allowed = None
        if masked:
            kpos = start + lax.broadcasted_iota(jnp.int32, (bk, 1), 0)
            allowed = (kdoc_ref[...] == qdoc_ref[...]) & (kpos < limit)
            allowed = jnp.concatenate([allowed] * heads, axis=1)
        update(kv_ref[:, :DH], kv_ref[:, DH:].T, qt_ref[...], fac, allowed, m_sc, l_sc, acc_sc)

    @pl.when(mode == 2)
    def _():
        step(False)

    @pl.when(mode == 1)
    def _():
        step(True)

    @pl.when(j == steps - 1)
    def _():
        for h in range(heads):
            cols = slice(h * rows, (h + 1) * rows)
            out = (acc_sc[:, cols] / l_sc[:, cols]).T.astype(o_ref.dtype)
            for c in range(copies):
                o_ref[c, :, h * DH:(h + 1) * DH] = out


def attend(plan, query_rows, kv_local, kv, query_doc, query_pos, factor, local_doc, key_doc,
           steps, bk, copies):
    rows, width = query_rows.shape
    heads = width // DH
    qt = query_rows.reshape(rows, heads, DH).transpose(2, 1, 0).reshape(DH, heads * rows)
    qdoc = query_doc.reshape(1, rows)
    fac = factor.reshape(1, rows)
    state = [
        jax.ShapeDtypeStruct((1, heads * rows), jnp.float32),
        jax.ShapeDtypeStruct((1, heads * rows), jnp.float32),
        jax.ShapeDtypeStruct((DH, heads * rows), jnp.float32),
    ]
    m0, l0, acc0 = pl.pallas_call(
        functools.partial(local_kernel, heads=heads),
        out_shape=state,
    )(qt, kv_local, qdoc, query_pos.reshape(1, rows), fac, local_doc.reshape(-1, 1),
      query_pos.reshape(-1, 1))

    def kv_map(j, p):
        return (pl.multiple_of(p[j], rows), 0)

    whole = lambda j, p: (0, 0)
    return pl.pallas_call(
        functools.partial(far_kernel, heads=heads, rows=rows, bk=bk, steps=steps,
                          copies=copies),
        out_shape=jax.ShapeDtypeStruct((copies, rows, width), jnp.bfloat16),
        grid_spec=pltpu.PrefetchScalarGridSpec(
            num_scalar_prefetch=1,
            grid=(steps,),
            in_specs=[
                pl.BlockSpec((DH, heads * rows), whole),
                pl.BlockSpec((pl.Element(bk), pl.Element(2 * DH)), kv_map),
                pl.BlockSpec((1, rows), whole),
                pl.BlockSpec((1, rows), whole),
                pl.BlockSpec((pl.Element(bk), pl.Element(1)), kv_map),
                pl.BlockSpec((1, heads * rows), whole),
                pl.BlockSpec((1, heads * rows), whole),
                pl.BlockSpec((DH, heads * rows), whole),
            ],
            out_specs=pl.BlockSpec((copies, rows, width), lambda j, p: (0, 0, 0)),
            scratch_shapes=[
                pltpu.VMEM((1, heads * rows), jnp.float32),
                pltpu.VMEM((1, heads * rows), jnp.float32),
                pltpu.VMEM((DH, heads * rows), jnp.float32),
            ],
        ),
        compiler_params=pltpu.CompilerParams(dimension_semantics=("arbitrary",)),
    )(plan, qt, kv, qdoc, fac, key_doc.reshape(-1, 1), m0, l0, acc0)


def body(queries, keys, values, doc_lengths):
    query_rows = queries[0]
    key_rows = keys[0]
    value_rows = values[0]
    lengths = doc_lengths[0]
    rows = query_rows.shape[0]
    cycle = lax.axis_size("ctx")
    count = rows * cycle
    base_len = count // 16
    position = lax.axis_index("ctx")
    first = position * rows
    ends = jnp.cumsum(lengths)
    starts = ends - lengths
    query_pos = first + jnp.arange(rows, dtype=jnp.int32)
    query_doc = doc_of(query_pos, ends)
    lookup = query_doc[:, None] == jnp.arange(DOCS, dtype=jnp.int32)[None, :]
    query_len = jnp.sum(jnp.where(lookup, lengths[None, :], 0), axis=1).astype(jnp.float32)
    factor = jnp.maximum(1.0, jnp.log(query_len) / math.log(float(base_len))) * (
        1.0 / math.sqrt(DH)
    )
    bk = min(BK, count)
    steps = max(1, max(-(-min(c * rows, MOST - 1) // bk) for c in range(cycle)))
    first_doc = jnp.sum((first >= ends).astype(jnp.int32))
    last_doc = jnp.sum((first + rows - 1 >= ends).astype(jnp.int32))
    doc_start = jnp.sum(jnp.where(jnp.arange(DOCS) == first_doc, starts, 0))
    need = (first - doc_start + bk - 1) // bk
    back = steps - jnp.arange(steps, dtype=jnp.int32)
    back = jnp.maximum(jnp.minimum(back, need), 1)
    limit = first - bk * (back - 1)
    raw = limit - bk
    start = jnp.maximum(raw, 0)
    active = (steps - jnp.arange(steps, dtype=jnp.int32)) <= need
    full = active & (raw >= doc_start) & (last_doc == first_doc)
    mode = jnp.where(full, 2, jnp.where(active, 1, 0))
    plan = jnp.concatenate([start, limit, mode]).astype(jnp.int32)
    kv_rows = jnp.concatenate([key_rows, value_rows], axis=1)
    kv = lax.all_gather(kv_rows, "ctx", axis=0, tiled=True)
    key_doc = doc_of(jnp.arange(count, dtype=jnp.int32), ends)
    sections = lax.axis_size("section")
    result = attend(
        plan, query_rows, kv_rows, kv, query_doc, query_pos, factor, query_doc, key_doc,
        steps, bk, sections,
    )
    share = lax.axis_size("mp")
    width = result.shape[2]
    got = lax.all_to_all(
        result.reshape(sections * rows, width), ("section", "mp"), 0, 1, tiled=True
    )
    here = lax.axis_index("section")
    behind = (here + sections - 1) % sections
    span_cols = share * width
    own = lax.dynamic_slice_in_dim(got, here * span_cols, span_cols, axis=1)
    moved = lax.dynamic_slice_in_dim(got, behind * span_cols, span_cols, axis=1)
    return (own[None], moved[None])


def solution(mesh):
    return jax.shard_map(
        body,
        mesh=mesh,
        in_specs=(
            P("section", "ctx", "mp"),
            P("section", "ctx", "mp"),
            P("section", "ctx", "mp"),
            P("section", None),
        ),
        out_specs=(P("section", ("ctx", "mp"), None), P("section", ("ctx", "mp"), None)),
        check_vma=False,
    )
```

```python
import functools
import math

import jax
import jax.numpy as jnp
from jax import lax
from jax.experimental import pallas as pl
from jax.experimental.pallas import tpu as pltpu
from jax.sharding import PartitionSpec as P

DH = 128
LOG2E = 1.4426950408889634
DOCS = 16
MOST = 4096
BK = 512


def doc_of(positions, ends):
    return jnp.sum((positions[:, None] >= ends[None, :]).astype(jnp.int32), axis=1)


def update(k, vt, qt, fac, allowed, m_ref, l_ref, acc_ref):
    s = jnp.dot(k, qt, preferred_element_type=jnp.float32)
    s = s * (fac * LOG2E)
    if allowed is not None:
        s = jnp.where(allowed, s, -1e30)
    m_old = m_ref[...]
    m_new = jnp.maximum(m_old, jnp.max(s, axis=0, keepdims=True))
    alpha = jnp.exp2(m_old - m_new)
    p = jnp.exp2(s - m_new)
    if allowed is not None:
        p = jnp.where(allowed, p, 0.0)
    l_ref[...] = alpha * l_ref[...] + jnp.sum(p, axis=0, keepdims=True)
    pv = jnp.dot(vt, p.astype(jnp.bfloat16), preferred_element_type=jnp.float32)
    acc_ref[...] = alpha * acc_ref[...] + pv
    m_ref[...] = m_new


def local_kernel(qt_ref, kv_ref, qdoc_ref, qpos_ref, fac_ref, kdoc_ref, kpos_ref,
                 m_ref, l_ref, acc_ref, *, heads):
    m_ref[...] = jnp.full(m_ref.shape, -1e30, jnp.float32)
    l_ref[...] = jnp.zeros(l_ref.shape, jnp.float32)
    acc_ref[...] = jnp.zeros(acc_ref.shape, jnp.float32)
    allowed = (kdoc_ref[...] == qdoc_ref[...]) & (kpos_ref[...] <= qpos_ref[...])
    allowed = jnp.concatenate([allowed] * heads, axis=1)
    fac = jnp.concatenate([fac_ref[...]] * heads, axis=1)
    update(kv_ref[:, :DH], kv_ref[:, DH:].T, qt_ref[...], fac, allowed, m_ref, l_ref, acc_ref)


def far_kernel(plan_ref, qt_ref, kv_ref, qdoc_ref, fac_ref, kdoc_ref, m0_ref, l0_ref, acc0_ref,
               o_ref, m_sc, l_sc, acc_sc, *, heads, rows, bk, steps, copies):
    j = pl.program_id(0)
    start = plan_ref[j]
    limit = plan_ref[steps + j]
    mode = plan_ref[2 * steps + j]

    @pl.when(j == 0)
    def _():
        m_sc[...] = jnp.full(m_sc.shape, -1e30, jnp.float32)
        l_sc[...] = jnp.zeros(l_sc.shape, jnp.float32)
        acc_sc[...] = jnp.zeros(acc_sc.shape, jnp.float32)

    def step(masked):
        fac = jnp.concatenate([fac_ref[...]] * heads, axis=1)
        allowed = None
        if masked:
            kpos = start + lax.broadcasted_iota(jnp.int32, (bk, 1), 0)
            allowed = (kdoc_ref[...] == qdoc_ref[...]) & (kpos < limit)
            allowed = jnp.concatenate([allowed] * heads, axis=1)
        update(kv_ref[:, :DH], kv_ref[:, DH:].T, qt_ref[...], fac, allowed, m_sc, l_sc, acc_sc)

    @pl.when(mode == 2)
    def _():
        step(False)

    @pl.when(mode == 1)
    def _():
        step(True)

    @pl.when(j == steps - 1)
    def _():
        inside = jnp.concatenate([qdoc_ref[...]] * heads, axis=1) == plan_ref[3 * steps]
        m_a = m0_ref[...]
        m_b = m_sc[...]
        m = jnp.where(inside, jnp.maximum(m_a, m_b), m_a)
        c_a = jnp.exp2(m_a - m)
        c_b = jnp.where(inside, jnp.exp2(m_b - m), 0.0)
        total = l0_ref[...] * c_a + l_sc[...] * c_b
        acc_sc[...] = acc0_ref[...] * c_a + acc_sc[...] * c_b
        l_sc[...] = total
        for h in range(heads):
            cols = slice(h * rows, (h + 1) * rows)
            out = (acc_sc[:, cols] / l_sc[:, cols]).T.astype(o_ref.dtype)
            for c in range(copies):
                o_ref[c, :, h * DH:(h + 1) * DH] = out


def attend(plan, query_rows, kv_local, kv, query_doc, query_pos, factor, local_doc, key_doc,
           steps, bk, copies):
    rows, width = query_rows.shape
    heads = width // DH
    qt = query_rows.reshape(rows, heads, DH).transpose(2, 1, 0).reshape(DH, heads * rows)
    qdoc = query_doc.reshape(1, rows)
    fac = factor.reshape(1, rows)
    state = [
        jax.ShapeDtypeStruct((1, heads * rows), jnp.float32),
        jax.ShapeDtypeStruct((1, heads * rows), jnp.float32),
        jax.ShapeDtypeStruct((DH, heads * rows), jnp.float32),
    ]
    m0, l0, acc0 = pl.pallas_call(
        functools.partial(local_kernel, heads=heads),
        out_shape=state,
    )(qt, kv_local, qdoc, query_pos.reshape(1, rows), fac, local_doc.reshape(-1, 1),
      query_pos.reshape(-1, 1))

    def kv_map(j, p):
        return (pl.multiple_of(p[j], rows), 0)

    whole = lambda j, p: (0, 0)
    return pl.pallas_call(
        functools.partial(far_kernel, heads=heads, rows=rows, bk=bk, steps=steps,
                          copies=copies),
        out_shape=jax.ShapeDtypeStruct((copies, rows, width), jnp.bfloat16),
        grid_spec=pltpu.PrefetchScalarGridSpec(
            num_scalar_prefetch=1,
            grid=(steps,),
            in_specs=[
                pl.BlockSpec((DH, heads * rows), whole),
                pl.BlockSpec((pl.Element(bk), pl.Element(2 * DH)), kv_map),
                pl.BlockSpec((1, rows), whole),
                pl.BlockSpec((1, rows), whole),
                pl.BlockSpec((pl.Element(bk), pl.Element(1)), kv_map),
                pl.BlockSpec((1, heads * rows), whole),
                pl.BlockSpec((1, heads * rows), whole),
                pl.BlockSpec((DH, heads * rows), whole),
            ],
            out_specs=pl.BlockSpec((copies, rows, width), lambda j, p: (0, 0, 0)),
            scratch_shapes=[
                pltpu.VMEM((1, heads * rows), jnp.float32),
                pltpu.VMEM((1, heads * rows), jnp.float32),
                pltpu.VMEM((DH, heads * rows), jnp.float32),
            ],
        ),
        compiler_params=pltpu.CompilerParams(dimension_semantics=("arbitrary",)),
    )(plan, qt, kv, qdoc, fac, key_doc.reshape(-1, 1), m0, l0, acc0)


def body(queries, keys, values, doc_lengths):
    query_rows = queries[0]
    key_rows = keys[0]
    value_rows = values[0]
    lengths = doc_lengths[0]
    rows = query_rows.shape[0]
    cycle = lax.axis_size("ctx")
    count = rows * cycle
    base_len = count // 16
    position = lax.axis_index("ctx")
    first = position * rows
    ends = jnp.cumsum(lengths)
    starts = ends - lengths
    query_pos = first + jnp.arange(rows, dtype=jnp.int32)
    query_doc = doc_of(query_pos, ends)
    lookup = query_doc[:, None] == jnp.arange(DOCS, dtype=jnp.int32)[None, :]
    query_len = jnp.sum(jnp.where(lookup, lengths[None, :], 0), axis=1).astype(jnp.float32)
    factor = jnp.maximum(1.0, jnp.log(query_len) / math.log(float(base_len))) * (
        1.0 / math.sqrt(DH)
    )
    bk = min(BK, count)
    steps = max(1, max(-(-min(c * rows, MOST - 1) // bk) for c in range(cycle)))
    first_doc = jnp.sum((first >= ends).astype(jnp.int32))
    doc_start = jnp.sum(jnp.where(jnp.arange(DOCS) == first_doc, starts, 0))
    need = (first - doc_start + bk - 1) // bk
    back = steps - jnp.arange(steps, dtype=jnp.int32)
    back = jnp.maximum(jnp.minimum(back, need), 1)
    limit = first - bk * (back - 1)
    raw = limit - bk
    start = jnp.maximum(raw, 0)
    active = (steps - jnp.arange(steps, dtype=jnp.int32)) <= need
    full = active & (raw >= doc_start)
    mode = jnp.where(full, 2, jnp.where(active, 1, 0))
    plan = jnp.concatenate([start, limit, mode, first_doc[None]]).astype(jnp.int32)
    kv_rows = jnp.concatenate([key_rows, value_rows], axis=1)
    kv = lax.all_gather(kv_rows, "ctx", axis=0, tiled=True)
    key_doc = doc_of(jnp.arange(count, dtype=jnp.int32), ends)
    sections = lax.axis_size("section")
    result = attend(
        plan, query_rows, kv_rows, kv, query_doc, query_pos, factor, query_doc, key_doc,
        steps, bk, sections,
    )
    share = lax.axis_size("mp")
    width = result.shape[2]
    got = lax.all_to_all(
        result.reshape(sections * rows, width), ("section", "mp"), 0, 1, tiled=True
    )
    here = lax.axis_index("section")
    behind = (here + sections - 1) % sections
    span_cols = share * width
    own = lax.dynamic_slice_in_dim(got, here * span_cols, span_cols, axis=1)
    moved = lax.dynamic_slice_in_dim(got, behind * span_cols, span_cols, axis=1)
    return (own[None], moved[None])


def solution(mesh):
    return jax.shard_map(
        body,
        mesh=mesh,
        in_specs=(
            P("section", "ctx", "mp"),
            P("section", "ctx", "mp"),
            P("section", "ctx", "mp"),
            P("section", None),
        ),
        out_specs=(P("section", ("ctx", "mp"), None), P("section", ("ctx", "mp"), None)),
        check_vma=False,
    )
```

```python
import functools
import math

import jax
import jax.numpy as jnp
from jax import lax
from jax.experimental import pallas as pl
from jax.experimental.pallas import tpu as pltpu
from jax.sharding import PartitionSpec as P

DH = 128
LOG2E = 1.4426950408889634
DOCS = 16
MOST = 4096
BK = 1024


def doc_of(positions, ends):
    return jnp.sum((positions[:, None] >= ends[None, :]).astype(jnp.int32), axis=1)


def update(k, vt, qt, fac, allowed, m_ref, l_ref, acc_ref):
    s = jnp.dot(k, qt, preferred_element_type=jnp.float32)
    s = s * (fac * LOG2E)
    if allowed is not None:
        s = jnp.where(allowed, s, -1e30)
    m_old = m_ref[...]
    m_new = jnp.maximum(m_old, jnp.max(s, axis=0, keepdims=True))
    alpha = jnp.exp2(m_old - m_new)
    p = jnp.exp2(s - m_new)
    if allowed is not None:
        p = jnp.where(allowed, p, 0.0)
    l_ref[...] = alpha * l_ref[...] + jnp.sum(p, axis=0, keepdims=True)
    pv = jnp.dot(vt, p.astype(jnp.bfloat16), preferred_element_type=jnp.float32)
    acc_ref[...] = alpha * acc_ref[...] + pv
    m_ref[...] = m_new


def local_kernel(qt_ref, kv_ref, qdoc_ref, qpos_ref, fac_ref, kdoc_ref, kpos_ref,
                 m_ref, l_ref, acc_ref, *, heads):
    m_ref[...] = jnp.full(m_ref.shape, -1e30, jnp.float32)
    l_ref[...] = jnp.zeros(l_ref.shape, jnp.float32)
    acc_ref[...] = jnp.zeros(acc_ref.shape, jnp.float32)
    allowed = (kdoc_ref[...] == qdoc_ref[...]) & (kpos_ref[...] <= qpos_ref[...])
    allowed = jnp.concatenate([allowed] * heads, axis=1)
    fac = jnp.concatenate([fac_ref[...]] * heads, axis=1)
    update(kv_ref[:, :DH], kv_ref[:, DH:].T, qt_ref[...], fac, allowed, m_ref, l_ref, acc_ref)


def far_kernel(plan_ref, qt_ref, kv_ref, qdoc_ref, fac_ref, kdoc_ref, m0_ref, l0_ref, acc0_ref,
               o_ref, m_sc, l_sc, acc_sc, *, heads, rows, bk, steps, copies):
    j = pl.program_id(0)
    start = plan_ref[j]
    limit = plan_ref[steps + j]
    mode = plan_ref[2 * steps + j]

    @pl.when(j == 0)
    def _():
        m_sc[...] = jnp.full(m_sc.shape, -1e30, jnp.float32)
        l_sc[...] = jnp.zeros(l_sc.shape, jnp.float32)
        acc_sc[...] = jnp.zeros(acc_sc.shape, jnp.float32)

    def step(masked):
        fac = jnp.concatenate([fac_ref[...]] * heads, axis=1)
        allowed = None
        if masked:
            kpos = start + lax.broadcasted_iota(jnp.int32, (bk, 1), 0)
            allowed = (kdoc_ref[...] == qdoc_ref[...]) & (kpos < limit)
            allowed = jnp.concatenate([allowed] * heads, axis=1)
        update(kv_ref[:, :DH], kv_ref[:, DH:].T, qt_ref[...], fac, allowed, m_sc, l_sc, acc_sc)

    @pl.when(mode == 2)
    def _():
        step(False)

    @pl.when(mode == 1)
    def _():
        step(True)

    @pl.when(j == steps - 1)
    def _():
        inside = jnp.concatenate([qdoc_ref[...]] * heads, axis=1) == plan_ref[3 * steps]
        m_a = m0_ref[...]
        m_b = m_sc[...]
        m = jnp.where(inside, jnp.maximum(m_a, m_b), m_a)
        c_a = jnp.exp2(m_a - m)
        c_b = jnp.where(inside, jnp.exp2(m_b - m), 0.0)
        total = l0_ref[...] * c_a + l_sc[...] * c_b
        acc_sc[...] = acc0_ref[...] * c_a + acc_sc[...] * c_b
        l_sc[...] = total
        for h in range(heads):
            cols = slice(h * rows, (h + 1) * rows)
            out = (acc_sc[:, cols] / l_sc[:, cols]).T.astype(o_ref.dtype)
            for c in range(copies):
                o_ref[c, :, h * DH:(h + 1) * DH] = out


def attend(plan, query_rows, kv_local, kv, query_doc, query_pos, factor, local_doc, key_doc,
           steps, bk, copies):
    rows, width = query_rows.shape
    heads = width // DH
    qt = query_rows.reshape(rows, heads, DH).transpose(2, 1, 0).reshape(DH, heads * rows)
    qdoc = query_doc.reshape(1, rows)
    fac = factor.reshape(1, rows)
    state = [
        jax.ShapeDtypeStruct((1, heads * rows), jnp.float32),
        jax.ShapeDtypeStruct((1, heads * rows), jnp.float32),
        jax.ShapeDtypeStruct((DH, heads * rows), jnp.float32),
    ]
    m0, l0, acc0 = pl.pallas_call(
        functools.partial(local_kernel, heads=heads),
        out_shape=state,
    )(qt, kv_local, qdoc, query_pos.reshape(1, rows), fac, local_doc.reshape(-1, 1),
      query_pos.reshape(-1, 1))

    def kv_map(j, p):
        return (pl.multiple_of(p[j], rows), 0)

    whole = lambda j, p: (0, 0)
    return pl.pallas_call(
        functools.partial(far_kernel, heads=heads, rows=rows, bk=bk, steps=steps,
                          copies=copies),
        out_shape=jax.ShapeDtypeStruct((copies, rows, width), jnp.bfloat16),
        grid_spec=pltpu.PrefetchScalarGridSpec(
            num_scalar_prefetch=1,
            grid=(steps,),
            in_specs=[
                pl.BlockSpec((DH, heads * rows), whole),
                pl.BlockSpec((pl.Element(bk), pl.Element(2 * DH)), kv_map),
                pl.BlockSpec((1, rows), whole),
                pl.BlockSpec((1, rows), whole),
                pl.BlockSpec((pl.Element(bk), pl.Element(1)), kv_map),
                pl.BlockSpec((1, heads * rows), whole),
                pl.BlockSpec((1, heads * rows), whole),
                pl.BlockSpec((DH, heads * rows), whole),
            ],
            out_specs=pl.BlockSpec((copies, rows, width), lambda j, p: (0, 0, 0)),
            scratch_shapes=[
                pltpu.VMEM((1, heads * rows), jnp.float32),
                pltpu.VMEM((1, heads * rows), jnp.float32),
                pltpu.VMEM((DH, heads * rows), jnp.float32),
            ],
        ),
        compiler_params=pltpu.CompilerParams(dimension_semantics=("arbitrary",)),
    )(plan, qt, kv, qdoc, fac, key_doc.reshape(-1, 1), m0, l0, acc0)


def body(queries, keys, values, doc_lengths):
    query_rows = queries[0]
    key_rows = keys[0]
    value_rows = values[0]
    lengths = doc_lengths[0]
    rows = query_rows.shape[0]
    cycle = lax.axis_size("ctx")
    count = rows * cycle
    base_len = count // 16
    position = lax.axis_index("ctx")
    first = position * rows
    ends = jnp.cumsum(lengths)
    starts = ends - lengths
    query_pos = first + jnp.arange(rows, dtype=jnp.int32)
    query_doc = doc_of(query_pos, ends)
    lookup = query_doc[:, None] == jnp.arange(DOCS, dtype=jnp.int32)[None, :]
    query_len = jnp.sum(jnp.where(lookup, lengths[None, :], 0), axis=1).astype(jnp.float32)
    factor = jnp.maximum(1.0, jnp.log(query_len) / math.log(float(base_len))) * (
        1.0 / math.sqrt(DH)
    )
    bk = min(BK, count)
    steps = max(1, max(-(-min(c * rows, MOST - 1) // bk) for c in range(cycle)))
    first_doc = jnp.sum((first >= ends).astype(jnp.int32))
    doc_start = jnp.sum(jnp.where(jnp.arange(DOCS) == first_doc, starts, 0))
    need = (first - doc_start + bk - 1) // bk
    back = steps - jnp.arange(steps, dtype=jnp.int32)
    back = jnp.maximum(jnp.minimum(back, need), 1)
    limit = first - bk * (back - 1)
    raw = limit - bk
    start = jnp.maximum(raw, 0)
    active = (steps - jnp.arange(steps, dtype=jnp.int32)) <= need
    full = active & (raw >= doc_start)
    mode = jnp.where(full, 2, jnp.where(active, 1, 0))
    plan = jnp.concatenate([start, limit, mode, first_doc[None]]).astype(jnp.int32)
    kv_rows = jnp.concatenate([key_rows, value_rows], axis=1)
    kv = lax.all_gather(kv_rows, "ctx", axis=0, tiled=True)
    key_doc = doc_of(jnp.arange(count, dtype=jnp.int32), ends)
    sections = lax.axis_size("section")
    result = attend(
        plan, query_rows, kv_rows, kv, query_doc, query_pos, factor, query_doc, key_doc,
        steps, bk, sections,
    )
    share = lax.axis_size("mp")
    width = result.shape[2]
    got = lax.all_to_all(
        result.reshape(sections * rows, width), ("section", "mp"), 0, 1, tiled=True
    )
    here = lax.axis_index("section")
    behind = (here + sections - 1) % sections
    span_cols = share * width
    own = lax.dynamic_slice_in_dim(got, here * span_cols, span_cols, axis=1)
    moved = lax.dynamic_slice_in_dim(got, behind * span_cols, span_cols, axis=1)
    return (own[None], moved[None])


def solution(mesh):
    return jax.shard_map(
        body,
        mesh=mesh,
        in_specs=(
            P("section", "ctx", "mp"),
            P("section", "ctx", "mp"),
            P("section", "ctx", "mp"),
            P("section", None),
        ),
        out_specs=(P("section", ("ctx", "mp"), None), P("section", ("ctx", "mp"), None)),
        check_vma=False,
    )
```

```python
import functools
import math

import jax
import jax.numpy as jnp
from jax import lax
from jax.experimental import pallas as pl
from jax.experimental.pallas import tpu as pltpu
from jax.sharding import PartitionSpec as P

DH = 128
LOG2E = 1.4426950408889634
DOCS = 16
MOST = 4096
BK = 2048


def doc_of(positions, ends):
    return jnp.sum((positions[:, None] >= ends[None, :]).astype(jnp.int32), axis=1)


def update(k, vt, qt, fac, allowed, m_ref, l_ref, acc_ref):
    s = jnp.dot(k, qt, preferred_element_type=jnp.float32)
    s = s * (fac * LOG2E)
    if allowed is not None:
        s = jnp.where(allowed, s, -1e30)
    m_old = m_ref[...]
    m_new = jnp.maximum(m_old, jnp.max(s, axis=0, keepdims=True))
    alpha = jnp.exp2(m_old - m_new)
    p = jnp.exp2(s - m_new)
    if allowed is not None:
        p = jnp.where(allowed, p, 0.0)
    l_ref[...] = alpha * l_ref[...] + jnp.sum(p, axis=0, keepdims=True)
    pv = jnp.dot(vt, p.astype(jnp.bfloat16), preferred_element_type=jnp.float32)
    acc_ref[...] = alpha * acc_ref[...] + pv
    m_ref[...] = m_new


def local_kernel(qt_ref, kv_ref, qdoc_ref, qpos_ref, fac_ref, kdoc_ref, kpos_ref,
                 m_ref, l_ref, acc_ref, *, heads):
    m_ref[...] = jnp.full(m_ref.shape, -1e30, jnp.float32)
    l_ref[...] = jnp.zeros(l_ref.shape, jnp.float32)
    acc_ref[...] = jnp.zeros(acc_ref.shape, jnp.float32)
    allowed = (kdoc_ref[...] == qdoc_ref[...]) & (kpos_ref[...] <= qpos_ref[...])
    allowed = jnp.concatenate([allowed] * heads, axis=1)
    fac = jnp.concatenate([fac_ref[...]] * heads, axis=1)
    update(kv_ref[:, :DH], kv_ref[:, DH:].T, qt_ref[...], fac, allowed, m_ref, l_ref, acc_ref)


def far_kernel(plan_ref, qt_ref, kv_ref, qdoc_ref, fac_ref, kdoc_ref, m0_ref, l0_ref, acc0_ref,
               o_ref, m_sc, l_sc, acc_sc, *, heads, rows, bk, steps, copies):
    j = pl.program_id(0)
    start = plan_ref[j]
    limit = plan_ref[steps + j]
    mode = plan_ref[2 * steps + j]

    @pl.when(j == 0)
    def _():
        m_sc[...] = jnp.full(m_sc.shape, -1e30, jnp.float32)
        l_sc[...] = jnp.zeros(l_sc.shape, jnp.float32)
        acc_sc[...] = jnp.zeros(acc_sc.shape, jnp.float32)

    def step(masked):
        fac = jnp.concatenate([fac_ref[...]] * heads, axis=1)
        allowed = None
        if masked:
            kpos = start + lax.broadcasted_iota(jnp.int32, (bk, 1), 0)
            allowed = (kdoc_ref[...] == qdoc_ref[...]) & (kpos < limit)
            allowed = jnp.concatenate([allowed] * heads, axis=1)
        update(kv_ref[:, :DH], kv_ref[:, DH:].T, qt_ref[...], fac, allowed, m_sc, l_sc, acc_sc)

    @pl.when(mode == 2)
    def _():
        step(False)

    @pl.when(mode == 1)
    def _():
        step(True)

    @pl.when(j == steps - 1)
    def _():
        inside = jnp.concatenate([qdoc_ref[...]] * heads, axis=1) == plan_ref[3 * steps]
        m_a = m0_ref[...]
        m_b = m_sc[...]
        m = jnp.where(inside, jnp.maximum(m_a, m_b), m_a)
        c_a = jnp.exp2(m_a - m)
        c_b = jnp.where(inside, jnp.exp2(m_b - m), 0.0)
        total = l0_ref[...] * c_a + l_sc[...] * c_b
        acc_sc[...] = acc0_ref[...] * c_a + acc_sc[...] * c_b
        l_sc[...] = total
        for h in range(heads):
            cols = slice(h * rows, (h + 1) * rows)
            out = (acc_sc[:, cols] / l_sc[:, cols]).T.astype(o_ref.dtype)
            for c in range(copies):
                o_ref[c, :, h * DH:(h + 1) * DH] = out


def attend(plan, query_rows, kv_local, kv, query_doc, query_pos, factor, local_doc, key_doc,
           steps, bk, copies):
    rows, width = query_rows.shape
    heads = width // DH
    qt = query_rows.reshape(rows, heads, DH).transpose(2, 1, 0).reshape(DH, heads * rows)
    qdoc = query_doc.reshape(1, rows)
    fac = factor.reshape(1, rows)
    state = [
        jax.ShapeDtypeStruct((1, heads * rows), jnp.float32),
        jax.ShapeDtypeStruct((1, heads * rows), jnp.float32),
        jax.ShapeDtypeStruct((DH, heads * rows), jnp.float32),
    ]
    m0, l0, acc0 = pl.pallas_call(
        functools.partial(local_kernel, heads=heads),
        out_shape=state,
    )(qt, kv_local, qdoc, query_pos.reshape(1, rows), fac, local_doc.reshape(-1, 1),
      query_pos.reshape(-1, 1))

    def kv_map(j, p):
        return (pl.multiple_of(p[j], rows), 0)

    whole = lambda j, p: (0, 0)
    return pl.pallas_call(
        functools.partial(far_kernel, heads=heads, rows=rows, bk=bk, steps=steps,
                          copies=copies),
        out_shape=jax.ShapeDtypeStruct((copies, rows, width), jnp.bfloat16),
        grid_spec=pltpu.PrefetchScalarGridSpec(
            num_scalar_prefetch=1,
            grid=(steps,),
            in_specs=[
                pl.BlockSpec((DH, heads * rows), whole),
                pl.BlockSpec((pl.Element(bk), pl.Element(2 * DH)), kv_map),
                pl.BlockSpec((1, rows), whole),
                pl.BlockSpec((1, rows), whole),
                pl.BlockSpec((pl.Element(bk), pl.Element(1)), kv_map),
                pl.BlockSpec((1, heads * rows), whole),
                pl.BlockSpec((1, heads * rows), whole),
                pl.BlockSpec((DH, heads * rows), whole),
            ],
            out_specs=pl.BlockSpec((copies, rows, width), lambda j, p: (0, 0, 0)),
            scratch_shapes=[
                pltpu.VMEM((1, heads * rows), jnp.float32),
                pltpu.VMEM((1, heads * rows), jnp.float32),
                pltpu.VMEM((DH, heads * rows), jnp.float32),
            ],
        ),
        compiler_params=pltpu.CompilerParams(dimension_semantics=("arbitrary",)),
    )(plan, qt, kv, qdoc, fac, key_doc.reshape(-1, 1), m0, l0, acc0)


def body(queries, keys, values, doc_lengths):
    query_rows = queries[0]
    key_rows = keys[0]
    value_rows = values[0]
    lengths = doc_lengths[0]
    rows = query_rows.shape[0]
    cycle = lax.axis_size("ctx")
    count = rows * cycle
    base_len = count // 16
    position = lax.axis_index("ctx")
    first = position * rows
    ends = jnp.cumsum(lengths)
    starts = ends - lengths
    query_pos = first + jnp.arange(rows, dtype=jnp.int32)
    query_doc = doc_of(query_pos, ends)
    lookup = query_doc[:, None] == jnp.arange(DOCS, dtype=jnp.int32)[None, :]
    query_len = jnp.sum(jnp.where(lookup, lengths[None, :], 0), axis=1).astype(jnp.float32)
    factor = jnp.maximum(1.0, jnp.log(query_len) / math.log(float(base_len))) * (
        1.0 / math.sqrt(DH)
    )
    bk = min(BK, count)
    steps = max(1, max(-(-min(c * rows, MOST - 1) // bk) for c in range(cycle)))
    first_doc = jnp.sum((first >= ends).astype(jnp.int32))
    doc_start = jnp.sum(jnp.where(jnp.arange(DOCS) == first_doc, starts, 0))
    need = (first - doc_start + bk - 1) // bk
    back = steps - jnp.arange(steps, dtype=jnp.int32)
    back = jnp.maximum(jnp.minimum(back, need), 1)
    limit = first - bk * (back - 1)
    raw = limit - bk
    start = jnp.maximum(raw, 0)
    active = (steps - jnp.arange(steps, dtype=jnp.int32)) <= need
    full = active & (raw >= doc_start)
    mode = jnp.where(full, 2, jnp.where(active, 1, 0))
    plan = jnp.concatenate([start, limit, mode, first_doc[None]]).astype(jnp.int32)
    kv_rows = jnp.concatenate([key_rows, value_rows], axis=1)
    kv = lax.all_gather(kv_rows, "ctx", axis=0, tiled=True)
    key_doc = doc_of(jnp.arange(count, dtype=jnp.int32), ends)
    sections = lax.axis_size("section")
    result = attend(
        plan, query_rows, kv_rows, kv, query_doc, query_pos, factor, query_doc, key_doc,
        steps, bk, sections,
    )
    share = lax.axis_size("mp")
    width = result.shape[2]
    got = lax.all_to_all(
        result.reshape(sections * rows, width), ("section", "mp"), 0, 1, tiled=True
    )
    here = lax.axis_index("section")
    behind = (here + sections - 1) % sections
    span_cols = share * width
    own = lax.dynamic_slice_in_dim(got, here * span_cols, span_cols, axis=1)
    moved = lax.dynamic_slice_in_dim(got, behind * span_cols, span_cols, axis=1)
    return (own[None], moved[None])


def solution(mesh):
    return jax.shard_map(
        body,
        mesh=mesh,
        in_specs=(
            P("section", "ctx", "mp"),
            P("section", "ctx", "mp"),
            P("section", "ctx", "mp"),
            P("section", None),
        ),
        out_specs=(P("section", ("ctx", "mp"), None), P("section", ("ctx", "mp"), None)),
        check_vma=False,
    )
```
